512 devices in a mesh: pix: 64 (over z, x), tm: 8 (over y, core).
Axes of the slice: x: 4, y: 4, z: 16, core: 2. Of those that a mesh axis runs over, the one named last changes fastest.
Arguments:
- movie: bfloat16 [131072, 2048], P('pix', 'tm'), may hold values from -6 to 6
- traces: bfloat16 [2048, 2048], P('pix', 'tm'), may hold values from 0 to 2
- footprints: bfloat16 [16384, 128], P('pix'), may hold values from 0 to 0.2
- slot_block: int32 [16384], P('pix'), may hold values from 0 to 15
- slot_neuron: int32 [16384], P('pix'), may hold values from 0 to 31
- bucket_fill: int32 [64, 64], P('pix'), may hold values from 1 to 4, as said below
Outputs:
- traces_new: bfloat16 [2048, 2048], P('pix', 'tm')
- footprints_new: float32 [16384, 128], P('pix')
The draws below stay inside these ranges and needn't reach their ends.
Inputs may be any that keep to these rules, and one draw needn't show every extreme that they name: `bucket_fill`: A tile has at most 4 used slots for one owner; in every draw some owner gets 4 from every tile, and every tile fills 4 for some owner.
All inputs are finite; a program needn't handle non-finite values.
Results may differ from the reference program's by a relative error of at most 0.0049.
Values may be sent and summed in bfloat16 or wider, within the bound.
No kernel may reach another device: no remote copies, remote signals or barrier semaphores. Data moves between devices by JAX's collectives and lax.ppermute only.
A program may use at most 64 MiB of HBM per device.

```python
import jax
import jax.numpy as jnp
from jax import lax

BLOCK = 128
NB_DEV = 16
SLOT_DEV = 256
NEUR_DEV = 32
PIX_DEV = 2048
PIXELS = 131072
FRAMES = 2048
NEURONS = 2048
CAP = 4
N_PIX = 64


def draw_bucket_fill(key, part):
    key_high, key_raw, key_col, key_dest = jax.random.split(key, 4)
    highest = jax.random.randint(key_high, (1, N_PIX), 2, 2 * CAP + 1)
    raw_fill = jax.random.randint(key_raw, (N_PIX, N_PIX), 1, highest)
    counts = jnp.minimum(raw_fill, CAP)
    columns = jnp.arange(N_PIX, dtype=jnp.int32)[None, :]
    forced_col = jax.random.randint(key_col, (N_PIX, 1), 0, N_PIX)
    counts = jnp.where(columns == forced_col, CAP, counts)
    full_dest = jax.random.randint(key_dest, (), 0, N_PIX)
    counts = jnp.where(columns == full_dest, CAP, counts)
    return counts.astype(jnp.int32)


def draw_footprints(key, part):
    key_keep, key_value = jax.random.split(jax.random.fold_in(key, 7))
    row_total = N_PIX * SLOT_DEV
    support = jax.random.randint(key_keep, (row_total, BLOCK), 0, 4 * SLOT_DEV) < 3 * NB_DEV
    values = jax.random.uniform(key_value, (row_total, BLOCK), jnp.float32, 0.0, 0.199)
    return jnp.where(support, values, 0.0).astype(jnp.bfloat16)


def set_ends(values, rng, low, top_value):
    dims = values.shape
    spot = [jax.random.randint(jax.random.fold_in(rng, axis), (), 0, dims[axis]) for axis in range(len(dims))]
    values = values.at[tuple(spot)].set(low)
    longest = dims.index(max(dims))
    spot[longest] = (spot[longest] + 1) % dims[longest]
    return values.at[tuple(spot)].set(top_value)


def levels(key, dims, cuts, low, high):
    def one(dim, shards_of):
        heights = jax.random.uniform(jax.random.fold_in(jax.random.fold_in(key, 6), dim), (shards_of,), jnp.float32, low / len(cuts), high / len(cuts))
        return jnp.repeat(jnp.exp(heights), dims[dim] // shards_of).reshape((-1,) + (1,) * (len(dims) - dim - 1))

    factor_of = one(*cuts[0])
    for cut in cuts[1:]:
        factor_of = factor_of * one(*cut)
    return factor_of


def normal_values(stream_key, extent, scale, most, cuts=(), kind=jnp.bfloat16):
    drawn = jax.random.normal(stream_key, extent, jnp.float32) * scale
    if len(cuts) > 0:
        drawn = levels(stream_key, extent, cuts, -0.22, 0.18) * drawn
    return jnp.clip(drawn, min=-most, max=most).astype(kind)


def setup_inputs(seed: int = 0) -> dict:
    splits = jax.random.split(jax.random.key(seed), 7)
    return {
        "movie": normal_values(splits[0], (PIXELS, FRAMES), 1.0, 6.0, ((0, 64), (1, 8))),
        "traces": jnp.clip(2.0 * jax.random.uniform(splits[1], (NEURONS, FRAMES), jnp.float32) ** levels(splits[1], (NEURONS, FRAMES), ((0, 64), (1, 8)), -0.2, 0.2), 0.0, 2.0).astype(jnp.bfloat16),
        "footprints": draw_footprints(jax.random.fold_in(splits[6], 71), 0),
        "slot_block": set_ends(jax.random.randint(splits[3], (N_PIX * SLOT_DEV,), 0, NB_DEV), jax.random.fold_in(splits[3], 1), 0, NB_DEV - 1).astype(jnp.int32),
        "slot_neuron": set_ends(jax.random.randint(splits[4], (N_PIX * SLOT_DEV,), 0, NEUR_DEV), jax.random.fold_in(splits[4], 1), 0, NEUR_DEV - 1).astype(jnp.int32),
        "bucket_fill": draw_bucket_fill(jax.random.fold_in(splits[6], 71), 0),
    }


def prepare_tile(foot, blocks, fill_row, bucket_of, position):
    usable = position < fill_row[bucket_of]
    masked = foot * usable[:, None].astype(jnp.bfloat16)
    block_pick = blocks[:, None] == jnp.arange(NB_DEV, dtype=jnp.int32)[None, :]
    dense_map = (block_pick.astype(jnp.bfloat16)[:, :, None] * masked[:, None, :]).reshape(SLOT_DEV, PIX_DEV)
    return usable, masked, block_pick, dense_map


def reference(movie, traces, footprints, slot_block, slot_neuron, bucket_fill):
    capacity = SLOT_DEV // N_PIX
    slot_index = jnp.arange(SLOT_DEV, dtype=jnp.int32)
    bucket_of = (slot_index // capacity).astype(jnp.int32)
    position = (slot_index % capacity).astype(jnp.int32)
    movie_tiles = movie.reshape(N_PIX, PIX_DEV, FRAMES)
    foot_tiles = footprints.reshape(N_PIX, SLOT_DEV, BLOCK)
    block_tiles = slot_block.reshape(N_PIX, SLOT_DEV)
    neuron_tiles = slot_neuron.reshape(N_PIX, SLOT_DEV)

    def first_pass(carry, tile):
        summed, power = carry
        pixels, foot, blocks, neurons, fill_row = tile
        usable, masked, block_pick, dense_map = prepare_tile(foot, blocks, fill_row, bucket_of, position)
        global_row = (bucket_of * NEUR_DEV + neurons).astype(jnp.int32)
        slot_traces = traces[global_row]
        rebuilt = jnp.dot(dense_map.T, slot_traces, preferred_element_type=jnp.float32)
        residual = (pixels.astype(jnp.float32) - rebuilt).astype(jnp.bfloat16)
        projection = jnp.dot(dense_map, residual, preferred_element_type=jnp.float32)
        slot_power = jnp.sum(masked.astype(jnp.float32) ** 2, axis=1)
        summed = summed.at[global_row].add(projection)
        power = power.at[global_row].add(slot_power)
        return (summed, power), None

    start = (jnp.zeros((NEURONS, FRAMES), jnp.float32), jnp.zeros((NEURONS,), jnp.float32))
    (summed, power), _ = lax.scan(first_pass, start, (movie_tiles, foot_tiles, block_tiles, neuron_tiles, bucket_fill))
    updated = jnp.maximum(0.0, traces.astype(jnp.float32) + summed / jnp.maximum(power, 0.5)[:, None]).astype(jnp.bfloat16)

    def second_pass(tile):
        pixels, foot, blocks, neurons, fill_row = tile
        usable, masked, block_pick, dense_map = prepare_tile(foot, blocks, fill_row, bucket_of, position)
        global_row = (bucket_of * NEUR_DEV + neurons).astype(jnp.int32)
        slot_traces = updated[global_row]
        rebuilt = jnp.dot(dense_map.T, slot_traces, preferred_element_type=jnp.float32)
        residual = (pixels.astype(jnp.float32) - rebuilt).astype(jnp.bfloat16)
        products = jnp.dot(residual, slot_traces.T, preferred_element_type=jnp.float32)
        numerator = jnp.einsum("bps,sb->sp", products.reshape(NB_DEV, BLOCK, SLOT_DEV), block_pick.astype(jnp.float32), precision=lax.Precision.HIGHEST)
        trace_power = jnp.sum(slot_traces.astype(jnp.float32) ** 2, axis=1)
        grown = jnp.maximum(0.0, masked.astype(jnp.float32) + numerator / (trace_power + 1e-6)[:, None])
        return jnp.where(usable[:, None], grown, 0.0)

    new_foot = lax.map(second_pass, (movie_tiles, foot_tiles, block_tiles, neuron_tiles, bucket_fill))
    return updated, new_foot.reshape(N_PIX * SLOT_DEV, BLOCK)
```

```python
import jax
import jax.numpy as jnp
from jax import lax
from jax.sharding import PartitionSpec as P

BLOCK = 128


def local(movie, traces, footprints, slot_block, slot_neuron, bucket_fill):
    pix_count = lax.axis_size("pix")
    tm_count = lax.axis_size("tm")
    slot_total = footprints.shape[0]
    capacity = slot_total // pix_count
    neur_local = traces.shape[0]
    frames = traces.shape[1]
    block_count = movie.shape[0] // BLOCK
    slot_index = jnp.arange(slot_total, dtype=jnp.int32)
    bucket_of = slot_index // capacity
    position = slot_index % capacity
    owner_match = bucket_of[:, None] == jnp.arange(pix_count, dtype=jnp.int32)[None, :]
    fill_slot = jnp.sum(jnp.where(owner_match, bucket_fill[0][None, :], 0), axis=1)
    usable = position < fill_slot
    masked = footprints * usable[:, None].astype(jnp.bfloat16)
    block_pick = slot_block[:, None] == jnp.arange(block_count, dtype=jnp.int32)[None, :]
    dense_map = (block_pick.astype(jnp.bfloat16)[:, :, None] * masked[:, None, :]).reshape(
        slot_total, block_count * BLOCK
    )
    asked = lax.all_to_all(
        slot_neuron.reshape(pix_count, capacity), "pix", split_axis=0, concat_axis=0, tiled=True
    )
    asked_flat = asked.reshape(slot_total)

    def slot_rows(source_rows):
        picked = jnp.take(source_rows, asked_flat, axis=0, mode="clip")
        got = lax.all_to_all(
            picked.reshape(pix_count, capacity, frames), "pix", split_axis=0, concat_axis=0, tiled=True
        )
        return got.reshape(slot_total, frames)

    def residual_of(slot_traces):
        rebuilt = lax.dot_general(
            dense_map, slot_traces, (((0,), (0,)), ((), ())), preferred_element_type=jnp.float32
        )
        return (movie.astype(jnp.float32) - rebuilt).astype(jnp.bfloat16)

    slot_traces = slot_rows(traces)
    residual = residual_of(slot_traces)
    projection = jnp.dot(dense_map, residual, preferred_element_type=jnp.float32)
    slot_power = jnp.sum(masked.astype(jnp.float32) ** 2, axis=1)
    power_row = jnp.pad(
        slot_power.reshape(pix_count, 1, capacity), ((0, 0), (0, 0), (0, frames - capacity))
    )
    sent = jnp.concatenate([projection.reshape(pix_count, capacity, frames), power_row], axis=1)
    got = lax.all_to_all(sent, "pix", split_axis=0, concat_axis=0, tiled=True)
    got_proj = got[:, :capacity, :].reshape(slot_total, frames)
    got_power = got[:, capacity, :capacity].reshape(slot_total)
    owner_pick = (jnp.arange(neur_local, dtype=jnp.int32)[:, None] == asked_flat[None, :]).astype(
        jnp.float32
    )
    summed = jnp.dot(owner_pick, got_proj, precision=lax.Precision.HIGHEST)
    power = jnp.dot(owner_pick, got_power, precision=lax.Precision.HIGHEST)
    updated = jnp.maximum(
        0.0, traces.astype(jnp.float32) + summed / jnp.maximum(power, 0.5)[:, None]
    ).astype(jnp.bfloat16)
    slot_updated = slot_rows(updated)
    residual_two = residual_of(slot_updated)
    products = lax.dot_general(
        residual_two, slot_updated, (((1,), (1,)), ((), ())), preferred_element_type=jnp.float32
    )
    numerator = jnp.einsum(
        "bps,sb->sp",
        products.reshape(block_count, BLOCK, slot_total),
        block_pick.astype(jnp.float32),
        precision=lax.Precision.HIGHEST,
    )
    trace_power = jnp.sum(slot_updated.astype(jnp.float32) ** 2, axis=1)
    pl_rows = slot_total // BLOCK
    stacked = jnp.concatenate([numerator, trace_power.reshape(pl_rows, BLOCK)], axis=0)
    rows = stacked.shape[0]
    chunk = -(-rows // tm_count)
    stacked = jnp.pad(stacked, ((0, chunk * tm_count - rows), (0, 0)))
    parts = lax.all_to_all(
        stacked.reshape(tm_count, chunk, BLOCK), "tm", split_axis=0, concat_axis=0, tiled=True
    )
    mine = jnp.sum(parts, axis=0, keepdims=True)
    whole = lax.all_to_all(
        jnp.broadcast_to(mine, (tm_count, chunk, BLOCK)), "tm", split_axis=0, concat_axis=0, tiled=True
    ).reshape(chunk * tm_count, BLOCK)
    numer_all = whole[:slot_total]
    power_all = whole[slot_total : slot_total + pl_rows].reshape(slot_total)
    grown = jnp.maximum(0.0, masked.astype(jnp.float32) + numer_all / (power_all + 1e-06)[:, None])
    return (updated, jnp.where(usable[:, None], grown, 0.0))


def solution(mesh):
    return jax.shard_map(
        local,
        mesh=mesh,
        in_specs=(
            P("pix", "tm"),
            P("pix", "tm"),
            P("pix", None),
            P("pix"),
            P("pix"),
            P("pix", None),
        ),
        out_specs=(P("pix", "tm"), P("pix", None)),
        check_vma=False,
    )
```

```python
import jax
import jax.numpy as jnp
from jax import lax
from jax.sharding import PartitionSpec as P

BLOCK = 128


def local(movie, traces, footprints, slot_block, slot_neuron, bucket_fill):
    pix_count = lax.axis_size("pix")
    tm_count = lax.axis_size("tm")
    slot_total = footprints.shape[0]
    capacity = slot_total // pix_count
    neur_local = traces.shape[0]
    frames = traces.shape[1]
    block_count = movie.shape[0] // BLOCK
    slot_index = jnp.arange(slot_total, dtype=jnp.int32)
    bucket_of = slot_index // capacity
    position = slot_index % capacity
    owner_match = bucket_of[:, None] == jnp.arange(pix_count, dtype=jnp.int32)[None, :]
    fill_slot = jnp.sum(jnp.where(owner_match, bucket_fill[0][None, :], 0), axis=1)
    usable = position < fill_slot
    masked = footprints * usable[:, None].astype(jnp.bfloat16)
    block_pick = slot_block[:, None] == jnp.arange(block_count, dtype=jnp.int32)[None, :]
    dense_map = (block_pick.astype(jnp.bfloat16)[:, :, None] * masked[:, None, :]).reshape(
        slot_total, block_count * BLOCK
    )
    slot_power = jnp.sum(masked.astype(jnp.float32) ** 2, axis=1)
    asked_and_power = lax.all_to_all(
        jnp.concatenate(
            [
                slot_neuron.astype(jnp.float32).reshape(pix_count, capacity),
                slot_power.reshape(pix_count, capacity),
            ],
            axis=1,
        ),
        "pix",
        split_axis=0,
        concat_axis=0,
        tiled=True,
    )
    asked_flat = asked_and_power[:, :capacity].astype(jnp.int32).reshape(slot_total)
    got_power = asked_and_power[:, capacity:].reshape(slot_total)

    def slot_rows(source_rows):
        picked = jnp.take(source_rows, asked_flat, axis=0, mode="clip")
        got = lax.all_to_all(
            picked.reshape(pix_count, capacity, frames), "pix", split_axis=0, concat_axis=0, tiled=True
        )
        return got.reshape(slot_total, frames)

    def residual_of(slot_traces):
        rebuilt = lax.dot_general(
            dense_map, slot_traces, (((0,), (0,)), ((), ())), preferred_element_type=jnp.float32
        )
        return (movie.astype(jnp.float32) - rebuilt).astype(jnp.bfloat16)

    slot_traces = slot_rows(traces)
    residual = residual_of(slot_traces)
    projection = jnp.dot(dense_map, residual, preferred_element_type=jnp.float32)
    got_proj = lax.all_to_all(
        projection.reshape(pix_count, capacity, frames), "pix", split_axis=0, concat_axis=0, tiled=True
    ).reshape(slot_total, frames)
    owner_pick = (jnp.arange(neur_local, dtype=jnp.int32)[:, None] == asked_flat[None, :]).astype(
        jnp.float32
    )
    summed = jnp.dot(owner_pick, got_proj, precision=lax.Precision.HIGHEST)
    power = jnp.dot(owner_pick, got_power, precision=lax.Precision.HIGHEST)
    updated = jnp.maximum(
        0.0, traces.astype(jnp.float32) + summed / jnp.maximum(power, 0.5)[:, None]
    ).astype(jnp.bfloat16)
    slot_updated = slot_rows(updated)
    residual_two = residual_of(slot_updated)
    products = lax.dot_general(
        residual_two, slot_updated, (((1,), (1,)), ((), ())), preferred_element_type=jnp.float32
    )
    numerator = jnp.einsum(
        "bps,sb->sp",
        products.reshape(block_count, BLOCK, slot_total),
        block_pick.astype(jnp.float32),
        precision=lax.Precision.HIGHEST,
    )
    trace_power = jnp.sum(slot_updated.astype(jnp.float32) ** 2, axis=1)
    pl_rows = slot_total // BLOCK
    stacked = jnp.concatenate([numerator, trace_power.reshape(pl_rows, BLOCK)], axis=0)
    rows = stacked.shape[0]
    chunk = -(-rows // tm_count)
    stacked = jnp.pad(stacked, ((0, chunk * tm_count - rows), (0, 0)))
    parts = lax.all_to_all(
        stacked.reshape(tm_count, chunk, BLOCK), "tm", split_axis=0, concat_axis=0, tiled=True
    )
    mine = jnp.sum(parts, axis=0, keepdims=True)
    whole = lax.all_to_all(
        jnp.broadcast_to(mine, (tm_count, chunk, BLOCK)), "tm", split_axis=0, concat_axis=0, tiled=True
    ).reshape(chunk * tm_count, BLOCK)
    numer_all = whole[:slot_total]
    power_all = whole[slot_total : slot_total + pl_rows].reshape(slot_total)
    grown = jnp.maximum(0.0, masked.astype(jnp.float32) + numer_all / (power_all + 1e-06)[:, None])
    return (updated, jnp.where(usable[:, None], grown, 0.0))


def solution(mesh):
    return jax.shard_map(
        local,
        mesh=mesh,
        in_specs=(
            P("pix", "tm"),
            P("pix", "tm"),
            P("pix", None),
            P("pix"),
            P("pix"),
            P("pix", None),
        ),
        out_specs=(P("pix", "tm"), P("pix", None)),
        check_vma=False,
    )
```

```python
import jax
import jax.numpy as jnp
from jax import lax
from jax.sharding import PartitionSpec as P

BLOCK = 128


def local(movie, traces, footprints, slot_block, slot_neuron, bucket_fill):
    pix_count = lax.axis_size("pix")
    tm_count = lax.axis_size("tm")
    slot_total = footprints.shape[0]
    capacity = slot_total // pix_count
    neur_local = traces.shape[0]
    frames = traces.shape[1]
    block_count = movie.shape[0] // BLOCK
    slot_index = jnp.arange(slot_total, dtype=jnp.int32)
    bucket_of = slot_index // capacity
    position = slot_index % capacity
    fill_slot = jnp.repeat(bucket_fill[0], capacity, total_repeat_length=slot_total)
    usable = position < fill_slot
    masked = footprints * usable[:, None].astype(jnp.bfloat16)
    block_pick = slot_block[:, None] == jnp.arange(block_count, dtype=jnp.int32)[None, :]
    dense_map = (block_pick.astype(jnp.bfloat16)[:, :, None] * masked[:, None, :]).reshape(
        slot_total, block_count * BLOCK
    )
    slot_power = jnp.sum(masked.astype(jnp.float32) ** 2, axis=1)
    asked_and_power = lax.all_to_all(
        jnp.concatenate(
            [
                slot_neuron.astype(jnp.float32).reshape(pix_count, capacity),
                slot_power.reshape(pix_count, capacity),
            ],
            axis=1,
        ),
        "pix",
        split_axis=0,
        concat_axis=0,
        tiled=True,
    )
    asked = asked_and_power[:, :capacity].astype(jnp.int32)
    asked_flat = asked.reshape(slot_total)
    row_pick = (asked[:, :, None] == jnp.arange(neur_local, dtype=jnp.int32)[None, None, :]).astype(
        jnp.bfloat16
    )
    got_power = asked_and_power[:, capacity:].reshape(slot_total)

    def slot_rows(source_rows):
        picked = jnp.einsum(
            "okn,nf->okf", row_pick, source_rows, preferred_element_type=jnp.float32
        ).astype(source_rows.dtype)
        got = lax.all_to_all(picked, "pix", split_axis=0, concat_axis=0, tiled=True)
        return got.reshape(slot_total, frames)

    def residual_of(slot_traces):
        rebuilt = lax.dot_general(
            dense_map, slot_traces, (((0,), (0,)), ((), ())), preferred_element_type=jnp.float32
        )
        return (movie.astype(jnp.float32) - rebuilt).astype(jnp.bfloat16)

    slot_traces = slot_rows(traces)
    residual = residual_of(slot_traces)
    projection = jnp.einsum(
        "okp,pf->okf",
        dense_map.reshape(pix_count, capacity, block_count * BLOCK),
        residual,
        preferred_element_type=jnp.float32,
    )
    got_proj = lax.all_to_all(
        projection, "pix", split_axis=0, concat_axis=0, tiled=True
    ).reshape(slot_total, frames)
    owner_pick = (jnp.arange(neur_local, dtype=jnp.int32)[:, None] == asked_flat[None, :]).astype(
        jnp.float32
    )
    summed = jnp.dot(owner_pick, got_proj, precision=lax.Precision.HIGHEST)
    power = jnp.dot(owner_pick, got_power, precision=lax.Precision.HIGHEST)
    updated = jnp.maximum(
        0.0, traces.astype(jnp.float32) + summed / jnp.maximum(power, 0.5)[:, None]
    ).astype(jnp.bfloat16)
    slot_updated = slot_rows(updated)
    residual_two = residual_of(slot_updated)
    products = lax.dot_general(
        slot_updated, residual_two, (((1,), (1,)), ((), ())), preferred_element_type=jnp.float32
    ).reshape(slot_total, block_count, BLOCK)
    numerator = jnp.sum(jnp.where(block_pick[:, :, None], products, 0.0), axis=1)
    trace_power = jnp.sum(slot_updated.astype(jnp.float32) ** 2, axis=1)
    pl_rows = slot_total // BLOCK
    stacked = jnp.concatenate([numerator, trace_power.reshape(pl_rows, BLOCK)], axis=0)
    rows = stacked.shape[0]
    chunk = -(-rows // tm_count)
    stacked = jnp.pad(stacked, ((0, chunk * tm_count - rows), (0, 0)))
    parts = lax.all_to_all(
        stacked.reshape(tm_count, chunk, BLOCK), "tm", split_axis=0, concat_axis=0, tiled=True
    )
    mine = jnp.sum(parts, axis=0, keepdims=True)
    whole = lax.all_to_all(
        jnp.broadcast_to(mine, (tm_count, chunk, BLOCK)), "tm", split_axis=0, concat_axis=0, tiled=True
    ).reshape(chunk * tm_count, BLOCK)
    numer_all = whole[:slot_total]
    power_all = whole[slot_total : slot_total + pl_rows].reshape(slot_total)
    grown = jnp.maximum(0.0, masked.astype(jnp.float32) + numer_all / (power_all + 1e-06)[:, None])
    return (updated, jnp.where(usable[:, None], grown, 0.0))


def solution(mesh):
    return jax.shard_map(
        local,
        mesh=mesh,
        in_specs=(
            P("pix", "tm"),
            P("pix", "tm"),
            P("pix", None),
            P("pix"),
            P("pix"),
            P("pix", None),
        ),
        out_specs=(P("pix", "tm"), P("pix", None)),
        check_vma=False,
    )
```

```python
import jax
import jax.numpy as jnp
from jax import lax
from jax.sharding import PartitionSpec as P

BLOCK = 128


def local(movie, traces, footprints, slot_block, slot_neuron, bucket_fill):
    pix_count = lax.axis_size("pix")
    tm_count = lax.axis_size("tm")
    slot_total = footprints.shape[0]
    capacity = slot_total // pix_count
    neur_local = traces.shape[0]
    frames = traces.shape[1]
    block_count = movie.shape[0] // BLOCK
    usable_op = jnp.arange(capacity, dtype=jnp.int32)[None, :] < bucket_fill[0][:, None]
    masked_op = footprints.reshape(pix_count, capacity, BLOCK) * usable_op[:, :, None].astype(
        jnp.bfloat16
    )
    power_op = jnp.sum(masked_op.astype(jnp.float32) ** 2, axis=2)
    usable = usable_op.reshape(slot_total)
    masked = masked_op.reshape(slot_total, BLOCK)
    block_pick = slot_block[:, None] == jnp.arange(block_count, dtype=jnp.int32)[None, :]
    dense_map = (block_pick.astype(jnp.bfloat16)[:, :, None] * masked[:, None, :]).reshape(
        slot_total, block_count * BLOCK
    )
    asked_and_power = lax.all_to_all(
        jnp.concatenate(
            [slot_neuron.reshape(pix_count, capacity).astype(jnp.float32), power_op], axis=1
        ),
        "pix",
        split_axis=0,
        concat_axis=0,
        tiled=True,
    )
    asked = asked_and_power[:, :capacity].astype(jnp.int32)
    asked_flat = asked.reshape(slot_total)
    row_pick = (asked[:, :, None] == jnp.arange(neur_local, dtype=jnp.int32)[None, None, :]).astype(
        jnp.bfloat16
    )
    got_power = asked_and_power[:, capacity:].reshape(slot_total)

    def slot_rows(source_rows):
        picked = jnp.einsum(
            "okn,nf->okf", row_pick, source_rows, preferred_element_type=jnp.float32
        ).astype(source_rows.dtype)
        got = lax.all_to_all(picked, "pix", split_axis=0, concat_axis=0, tiled=True)
        return got.reshape(slot_total, frames)

    def residual_of(slot_traces):
        rebuilt = lax.dot_general(
            dense_map, slot_traces, (((0,), (0,)), ((), ())), preferred_element_type=jnp.float32
        )
        return (movie.astype(jnp.float32) - rebuilt).astype(jnp.bfloat16)

    slot_traces = slot_rows(traces)
    residual = residual_of(slot_traces)
    projection = jnp.einsum(
        "okp,pf->okf",
        dense_map.reshape(pix_count, capacity, block_count * BLOCK),
        residual,
        preferred_element_type=jnp.float32,
    )
    got_proj = lax.all_to_all(
        projection, "pix", split_axis=0, concat_axis=0, tiled=True
    ).reshape(slot_total, frames)
    owner_pick = (jnp.arange(neur_local, dtype=jnp.int32)[:, None] == asked_flat[None, :]).astype(
        jnp.float32
    )
    summed = jnp.dot(owner_pick, got_proj, precision=lax.Precision.HIGHEST)
    power = jnp.dot(owner_pick, got_power, precision=lax.Precision.HIGHEST)
    updated = jnp.maximum(
        0.0, traces.astype(jnp.float32) + summed / jnp.maximum(power, 0.5)[:, None]
    ).astype(jnp.bfloat16)
    slot_updated = slot_rows(updated)
    residual_two = residual_of(slot_updated)
    products = lax.dot_general(
        slot_updated, residual_two, (((1,), (1,)), ((), ())), preferred_element_type=jnp.float32
    ).reshape(slot_total, block_count, BLOCK)
    numerator = jnp.sum(jnp.where(block_pick[:, :, None], products, 0.0), axis=1)
    trace_power = jnp.sum(slot_updated.astype(jnp.float32) ** 2, axis=1)
    pl_rows = slot_total // BLOCK
    stacked = jnp.concatenate([numerator, trace_power.reshape(pl_rows, BLOCK)], axis=0)
    rows = stacked.shape[0]
    chunk = -(-rows // tm_count)
    stacked = jnp.pad(stacked, ((0, chunk * tm_count - rows), (0, 0)))
    parts = lax.all_to_all(
        stacked.reshape(tm_count, chunk, BLOCK), "tm", split_axis=0, concat_axis=0, tiled=True
    )
    mine = jnp.sum(parts, axis=0, keepdims=True)
    whole = lax.all_to_all(
        jnp.broadcast_to(mine, (tm_count, chunk, BLOCK)), "tm", split_axis=0, concat_axis=0, tiled=True
    ).reshape(chunk * tm_count, BLOCK)
    numer_all = whole[:slot_total]
    power_all = whole[slot_total : slot_total + pl_rows].reshape(slot_total)
    grown = jnp.maximum(0.0, masked.astype(jnp.float32) + numer_all / (power_all + 1e-06)[:, None])
    return (updated, jnp.where(usable[:, None], grown, 0.0))


def solution(mesh):
    return jax.shard_map(
        local,
        mesh=mesh,
        in_specs=(
            P("pix", "tm"),
            P("pix", "tm"),
            P("pix", None),
            P("pix"),
            P("pix"),
            P("pix", None),
        ),
        out_specs=(P("pix", "tm"), P("pix", None)),
        check_vma=False,
    )
```

```python
import jax
import jax.numpy as jnp
from jax import lax
from jax.sharding import PartitionSpec as P

BLOCK = 128


def local(movie, traces, footprints, slot_block, slot_neuron, bucket_fill):
    pix_count = lax.axis_size("pix")
    tm_count = lax.axis_size("tm")
    slot_total = footprints.shape[0]
    capacity = slot_total // pix_count
    neur_local = traces.shape[0]
    frames = traces.shape[1]
    block_count = movie.shape[0] // BLOCK
    usable_op = jnp.arange(capacity, dtype=jnp.int32)[None, :] < bucket_fill[0][:, None]
    masked_op = footprints.reshape(pix_count, capacity, BLOCK) * usable_op[:, :, None].astype(
        jnp.bfloat16
    )
    power_op = jnp.where(
        usable_op,
        jnp.sum(footprints.reshape(pix_count, capacity, BLOCK).astype(jnp.float32) ** 2, axis=2),
        0.0,
    )
    usable = usable_op.reshape(slot_total)
    masked = masked_op.reshape(slot_total, BLOCK)
    block_pick = slot_block[:, None] == jnp.arange(block_count, dtype=jnp.int32)[None, :]
    dense_map = (block_pick.astype(jnp.bfloat16)[:, :, None] * masked[:, None, :]).reshape(
        slot_total, block_count * BLOCK
    )
    asked_and_power = lax.all_to_all(
        jnp.concatenate(
            [slot_neuron.reshape(pix_count, capacity).astype(jnp.float32), power_op], axis=1
        ),
        "pix",
        split_axis=0,
        concat_axis=0,
        tiled=True,
    )
    asked = asked_and_power[:, :capacity].astype(jnp.int32)
    asked_flat = asked.reshape(slot_total)
    row_pick = (asked[:, :, None] == jnp.arange(neur_local, dtype=jnp.int32)[None, None, :]).astype(
        jnp.bfloat16
    )
    got_power = asked_and_power[:, capacity:].reshape(slot_total)

    def slot_rows(source_rows):
        picked = jnp.einsum(
            "okn,nf->okf", row_pick, source_rows, preferred_element_type=jnp.float32
        ).astype(source_rows.dtype)
        got = lax.all_to_all(picked, "pix", split_axis=0, concat_axis=0, tiled=True)
        return got.reshape(slot_total, frames)

    def residual_of(slot_traces):
        rebuilt = lax.dot_general(
            dense_map, slot_traces, (((0,), (0,)), ((), ())), preferred_element_type=jnp.float32
        )
        return (movie.astype(jnp.float32) - rebuilt).astype(jnp.bfloat16)

    slot_traces = slot_rows(traces)
    residual = residual_of(slot_traces)
    projection = jnp.einsum(
        "okp,pf->okf",
        dense_map.reshape(pix_count, capacity, block_count * BLOCK),
        residual,
        preferred_element_type=jnp.float32,
    )
    got_proj = lax.all_to_all(
        projection, "pix", split_axis=0, concat_axis=0, tiled=True
    ).reshape(slot_total, frames)
    owner_pick = (jnp.arange(neur_local, dtype=jnp.int32)[:, None] == asked_flat[None, :]).astype(
        jnp.float32
    )
    summed = jnp.dot(owner_pick, got_proj, precision=lax.Precision.HIGHEST)
    power = jnp.dot(owner_pick, got_power, precision=lax.Precision.HIGHEST)
    updated = jnp.maximum(
        0.0, traces.astype(jnp.float32) + summed / jnp.maximum(power, 0.5)[:, None]
    ).astype(jnp.bfloat16)
    slot_updated = slot_rows(updated)
    residual_two = residual_of(slot_updated)
    products = lax.dot_general(
        slot_updated, residual_two, (((1,), (1,)), ((), ())), preferred_element_type=jnp.float32
    ).reshape(slot_total, block_count, BLOCK)
    numerator = jnp.sum(jnp.where(block_pick[:, :, None], products, 0.0), axis=1)
    trace_power = jnp.sum(slot_updated.astype(jnp.float32) ** 2, axis=1)
    pl_rows = slot_total // BLOCK
    stacked = jnp.concatenate([numerator, trace_power.reshape(pl_rows, BLOCK)], axis=0)
    rows = stacked.shape[0]
    chunk = -(-rows // tm_count)
    stacked = jnp.pad(stacked, ((0, chunk * tm_count - rows), (0, 0)))
    parts = lax.all_to_all(
        stacked.reshape(tm_count, chunk, BLOCK), "tm", split_axis=0, concat_axis=0, tiled=True
    )
    mine = jnp.sum(parts, axis=0, keepdims=True)
    whole = lax.all_to_all(
        jnp.broadcast_to(mine, (tm_count, chunk, BLOCK)), "tm", split_axis=0, concat_axis=0, tiled=True
    ).reshape(chunk * tm_count, BLOCK)
    numer_all = whole[:slot_total]
    power_all = whole[slot_total : slot_total + pl_rows].reshape(slot_total)
    grown = jnp.maximum(0.0, masked.astype(jnp.float32) + numer_all / (power_all + 1e-06)[:, None])
    return (updated, jnp.where(usable[:, None], grown, 0.0))


def solution(mesh):
    return jax.shard_map(
        local,
        mesh=mesh,
        in_specs=(
            P("pix", "tm"),
            P("pix", "tm"),
            P("pix", None),
            P("pix"),
            P("pix"),
            P("pix", None),
        ),
        out_specs=(P("pix", "tm"), P("pix", None)),
        check_vma=False,
    )
```

```python
import jax
import jax.numpy as jnp
from jax import lax
from jax.sharding import PartitionSpec as P

BLOCK = 128


def local(movie, traces, footprints, slot_block, slot_neuron, bucket_fill):
    pix_count = lax.axis_size("pix")
    tm_count = lax.axis_size("tm")
    slot_total = footprints.shape[0]
    capacity = slot_total // pix_count
    neur_local = traces.shape[0]
    frames = traces.shape[1]
    block_count = movie.shape[0] // BLOCK
    usable_op = jnp.arange(capacity, dtype=jnp.int32)[None, :] < bucket_fill[0][:, None]
    masked_op = footprints.reshape(pix_count, capacity, BLOCK) * usable_op[:, :, None].astype(
        jnp.bfloat16
    )
    power_op = jnp.sum(masked_op.astype(jnp.float32) ** 2, axis=2)
    usable = usable_op.reshape(slot_total)
    masked = masked_op.reshape(slot_total, BLOCK)
    block_pick = slot_block[:, None] == jnp.arange(block_count, dtype=jnp.int32)[None, :]
    dense_map = (block_pick.astype(jnp.bfloat16)[:, :, None] * masked[:, None, :]).reshape(
        slot_total, block_count * BLOCK
    )
    asked_and_power = lax.all_to_all(
        jnp.concatenate(
            [slot_neuron.reshape(pix_count, capacity).astype(jnp.float32), power_op], axis=1
        ),
        "pix",
        split_axis=0,
        concat_axis=0,
        tiled=True,
    )
    asked = asked_and_power[:, :capacity].astype(jnp.int32)
    asked_flat = asked.reshape(slot_total)
    row_pick = (asked[:, :, None] == jnp.arange(neur_local, dtype=jnp.int32)[None, None, :]).astype(
        jnp.bfloat16
    )
    got_power = asked_and_power[:, capacity:].reshape(slot_total)

    def slot_rows(source_rows):
        picked = jnp.einsum(
            "okn,nf->okf", row_pick, source_rows, preferred_element_type=jnp.float32
        ).astype(source_rows.dtype)
        got = lax.all_to_all(picked, "pix", split_axis=0, concat_axis=0, tiled=True)
        return got.reshape(slot_total, frames)

    def residual_of(slot_traces):
        rebuilt = lax.dot_general(
            dense_map, slot_traces, (((0,), (0,)), ((), ())), preferred_element_type=jnp.float32
        )
        return (movie.astype(jnp.float32) - rebuilt).astype(jnp.bfloat16)

    slot_traces = slot_rows(traces)
    residual = residual_of(slot_traces)
    projection = jnp.einsum(
        "okp,pf->okf",
        dense_map.reshape(pix_count, capacity, block_count * BLOCK),
        residual,
        preferred_element_type=jnp.float32,
    )
    got_proj = lax.all_to_all(
        projection, "pix", split_axis=0, concat_axis=0, tiled=True
    ).reshape(slot_total, frames)
    owner_pick = (jnp.arange(neur_local, dtype=jnp.int32)[:, None] == asked_flat[None, :]).astype(
        jnp.float32
    )
    summed = jnp.dot(owner_pick, got_proj, precision=lax.Precision.HIGHEST)
    power = jnp.dot(owner_pick, got_power, precision=lax.Precision.HIGHEST)
    updated = jnp.maximum(
        0.0, traces.astype(jnp.float32) + summed / jnp.maximum(power, 0.5)[:, None]
    ).astype(jnp.bfloat16)
    slot_updated = slot_rows(updated)
    residual_two = residual_of(slot_updated)
    products = lax.dot_general(
        slot_updated, residual_two, (((1,), (1,)), ((), ())), preferred_element_type=jnp.float32
    ).reshape(slot_total, block_count, BLOCK)
    numerator = jnp.sum(jnp.where(block_pick[:, :, None], products, 0.0), axis=1)
    trace_power = jnp.sum(slot_updated.astype(jnp.float32) ** 2, axis=1)
    per = slot_total // tm_count
    stacked = jnp.concatenate(
        [
            numerator.reshape(tm_count, per, BLOCK),
            jnp.pad(trace_power.reshape(tm_count, 1, per), ((0, 0), (0, 0), (0, BLOCK - per))),
        ],
        axis=1,
    )
    parts = lax.all_to_all(stacked, "tm", split_axis=0, concat_axis=0, tiled=True)
    mine = jnp.sum(parts, axis=0)
    first = lax.axis_index("tm") * per
    masked_mine = lax.dynamic_slice_in_dim(masked, first, per, 0)
    usable_mine = lax.dynamic_slice_in_dim(usable, first, per, 0)
    grown = jnp.maximum(
        0.0, masked_mine.astype(jnp.float32) + mine[:per] / (mine[per, :per] + 1e-06)[:, None]
    )
    grown = jnp.where(usable_mine[:, None], grown, 0.0)
    whole = lax.all_to_all(
        jnp.broadcast_to(grown[None], (tm_count, per, BLOCK)), "tm", split_axis=0, concat_axis=0, tiled=True
    ).reshape(slot_total, BLOCK)
    return (updated, whole)


def solution(mesh):
    return jax.shard_map(
        local,
        mesh=mesh,
        in_specs=(
            P("pix", "tm"),
            P("pix", "tm"),
            P("pix", None),
            P("pix"),
            P("pix"),
            P("pix", None),
        ),
        out_specs=(P("pix", "tm"), P("pix", None)),
        check_vma=False,
    )
```

```python
import jax
import jax.numpy as jnp
from jax import lax
from jax.sharding import PartitionSpec as P

BLOCK = 128


def local(movie, traces, footprints, slot_block, slot_neuron, bucket_fill):
    pix_count = lax.axis_size("pix")
    tm_count = lax.axis_size("tm")
    slot_total = footprints.shape[0]
    capacity = slot_total // pix_count
    neur_local = traces.shape[0]
    frames = traces.shape[1]
    block_count = movie.shape[0] // BLOCK
    usable_op = jnp.arange(capacity, dtype=jnp.int32)[None, :] < bucket_fill[0][:, None]
    masked_op = footprints.reshape(pix_count, capacity, BLOCK) * usable_op[:, :, None].astype(
        jnp.bfloat16
    )
    power_op = jnp.sum(masked_op.astype(jnp.float32) ** 2, axis=2)
    usable = usable_op.reshape(slot_total)
    masked = masked_op.reshape(slot_total, BLOCK)
    block_pick = slot_block[:, None] == jnp.arange(block_count, dtype=jnp.int32)[None, :]
    dense_map = (block_pick.astype(jnp.bfloat16)[:, :, None] * masked[:, None, :]).reshape(
        slot_total, block_count * BLOCK
    )
    asked_and_power = lax.all_to_all(
        jnp.concatenate(
            [slot_neuron.reshape(pix_count, capacity).astype(jnp.float32), power_op], axis=1
        ),
        "pix",
        split_axis=0,
        concat_axis=0,
        tiled=True,
    )
    asked = asked_and_power[:, :capacity].astype(jnp.int32)
    asked_flat = asked.reshape(slot_total)
    row_pick = (asked[:, :, None] == jnp.arange(neur_local, dtype=jnp.int32)[None, None, :]).astype(
        jnp.bfloat16
    )
    got_power = asked_and_power[:, capacity:].reshape(slot_total)

    def slot_rows(source_rows):
        picked = jnp.einsum(
            "okn,nf->okf", row_pick, source_rows, preferred_element_type=jnp.float32
        ).astype(source_rows.dtype)
        got = lax.all_to_all(picked, "pix", split_axis=0, concat_axis=0, tiled=True)
        return got.reshape(slot_total, frames)

    def residual_of(slot_traces):
        rebuilt = lax.dot_general(
            dense_map, slot_traces, (((0,), (0,)), ((), ())), preferred_element_type=jnp.float32
        )
        return (movie.astype(jnp.float32) - rebuilt).astype(jnp.bfloat16)

    slot_traces = slot_rows(traces)
    residual = residual_of(slot_traces)
    projection = jnp.einsum(
        "okp,pf->okf",
        dense_map.reshape(pix_count, capacity, block_count * BLOCK),
        residual,
        preferred_element_type=jnp.float32,
    )
    got_proj = lax.all_to_all(
        projection, "pix", split_axis=0, concat_axis=0, tiled=True
    ).reshape(slot_total, frames)
    owner_pick = (jnp.arange(neur_local, dtype=jnp.int32)[:, None] == asked_flat[None, :]).astype(
        jnp.float32
    )
    summed = jnp.dot(owner_pick, got_proj, precision=lax.Precision.HIGHEST)
    power = jnp.dot(owner_pick, got_power, precision=lax.Precision.HIGHEST)
    updated = jnp.maximum(
        0.0, traces.astype(jnp.float32) + summed / jnp.maximum(power, 0.5)[:, None]
    ).astype(jnp.bfloat16)
    slot_updated = slot_rows(updated)
    residual_two = residual_of(slot_updated)
    products = lax.dot_general(
        slot_updated, residual_two, (((1,), (1,)), ((), ())), preferred_element_type=jnp.float32
    ).reshape(slot_total, block_count, BLOCK)
    numerator = jnp.sum(jnp.where(block_pick[:, :, None], products, 0.0), axis=1)
    trace_power = jnp.sum(slot_updated.astype(jnp.float32) ** 2, axis=1)
    per = slot_total // tm_count
    stacked = jnp.concatenate(
        [
            numerator.reshape(tm_count, per, BLOCK),
            jnp.concatenate(
                [
                    trace_power.reshape(tm_count, 1, per),
                    jnp.broadcast_to(
                        0.0 * trace_power[0], (tm_count, 1, BLOCK - per - 1)
                    ),
                    jnp.arange(tm_count, dtype=jnp.float32)[:, None, None] + 0.0 * trace_power[0],
                ],
                axis=2,
            ),
        ],
        axis=1,
    )
    parts = lax.all_to_all(stacked, "tm", split_axis=0, concat_axis=0, tiled=True)
    mine = jnp.sum(parts, axis=0)
    first = parts[0, per, BLOCK - 1].astype(jnp.int32) * per
    masked_mine = lax.dynamic_slice_in_dim(masked, first, per, 0)
    usable_mine = lax.dynamic_slice_in_dim(usable, first, per, 0)
    grown = jnp.maximum(
        0.0, masked_mine.astype(jnp.float32) + mine[:per] / (mine[per, :per] + 1e-06)[:, None]
    )
    grown = jnp.where(usable_mine[:, None], grown, 0.0)
    whole = lax.all_to_all(
        jnp.broadcast_to(grown[None], (tm_count, per, BLOCK)), "tm", split_axis=0, concat_axis=0, tiled=True
    ).reshape(slot_total, BLOCK)
    return (updated, whole)


def solution(mesh):
    return jax.shard_map(
        local,
        mesh=mesh,
        in_specs=(
            P("pix", "tm"),
            P("pix", "tm"),
            P("pix", None),
            P("pix"),
            P("pix"),
            P("pix", None),
        ),
        out_specs=(P("pix", "tm"), P("pix", None)),
        check_vma=False,
    )
```

```python
import jax
import jax.numpy as jnp
from jax import lax
from jax.experimental import pallas as pl
from jax.experimental.pallas import tpu as pltpu
from jax.sharding import PartitionSpec as P

BLOCK = 128
CHUNK = 256


def first_pass_kernel(map_t_ref, map_ref, traces_ref, movie_ref, out_ref):
    acc = jnp.zeros(out_ref.shape, jnp.float32)
    for c in range(movie_ref.shape[0] // CHUNK):
        rows = pl.ds(c * CHUNK, CHUNK)
        rebuilt = jnp.dot(map_t_ref[rows, :], traces_ref[...], preferred_element_type=jnp.float32)
        residual = (movie_ref[rows, :].astype(jnp.float32) - rebuilt).astype(jnp.bfloat16)
        acc = acc + jnp.dot(map_ref[:, rows], residual, preferred_element_type=jnp.float32)
    out_ref[...] = acc


def first_pass(dense_map, slot_traces, movie):
    slots, pixels = dense_map.shape
    frames = movie.shape[1]
    return pl.pallas_call(
        first_pass_kernel,
        out_shape=jax.ShapeDtypeStruct((slots, frames), jnp.float32),
        in_specs=[pl.BlockSpec(memory_space=pltpu.VMEM)] * 4,
        out_specs=pl.BlockSpec(memory_space=pltpu.VMEM),
        cost_estimate=pl.CostEstimate(
            flops=4 * slots * pixels * frames,
            bytes_accessed=2 * (2 * slots * pixels + slots * frames + pixels * frames) + 4 * slots * frames,
            transcendentals=0,
        ),
    )(dense_map.T, dense_map, slot_traces, movie)


def local(movie, traces, footprints, slot_block, slot_neuron, bucket_fill):
    pix_count = lax.axis_size("pix")
    tm_count = lax.axis_size("tm")
    slot_total = footprints.shape[0]
    capacity = slot_total // pix_count
    neur_local = traces.shape[0]
    frames = traces.shape[1]
    block_count = movie.shape[0] // BLOCK
    usable_op = jnp.arange(capacity, dtype=jnp.int32)[None, :] < bucket_fill[0][:, None]
    masked_op = footprints.reshape(pix_count, capacity, BLOCK) * usable_op[:, :, None].astype(
        jnp.bfloat16
    )
    power_op = jnp.sum(masked_op.astype(jnp.float32) ** 2, axis=2)
    usable = usable_op.reshape(slot_total)
    masked = masked_op.reshape(slot_total, BLOCK)
    block_pick = slot_block[:, None] == jnp.arange(block_count, dtype=jnp.int32)[None, :]
    dense_map = (block_pick.astype(jnp.bfloat16)[:, :, None] * masked[:, None, :]).reshape(
        slot_total, block_count * BLOCK
    )
    asked_and_power = lax.all_to_all(
        jnp.concatenate(
            [slot_neuron.reshape(pix_count, capacity).astype(jnp.float32), power_op], axis=1
        ),
        "pix",
        split_axis=0,
        concat_axis=0,
        tiled=True,
    )
    asked = asked_and_power[:, :capacity].astype(jnp.int32)
    asked_flat = asked.reshape(slot_total)
    row_pick = (asked[:, :, None] == jnp.arange(neur_local, dtype=jnp.int32)[None, None, :]).astype(
        jnp.bfloat16
    )
    got_power = asked_and_power[:, capacity:].reshape(slot_total)

    def slot_rows(source_rows):
        picked = jnp.einsum(
            "okn,nf->okf", row_pick, source_rows, preferred_element_type=jnp.float32
        ).astype(source_rows.dtype)
        got = lax.all_to_all(picked, "pix", split_axis=0, concat_axis=0, tiled=True)
        return got.reshape(slot_total, frames)

    def residual_of(slot_traces):
        rebuilt = lax.dot_general(
            dense_map, slot_traces, (((0,), (0,)), ((), ())), preferred_element_type=jnp.float32
        )
        return (movie.astype(jnp.float32) - rebuilt).astype(jnp.bfloat16)

    slot_traces = slot_rows(traces)
    projection = first_pass(dense_map, slot_traces, movie).reshape(pix_count, capacity, frames)
    got_proj = lax.all_to_all(
        projection, "pix", split_axis=0, concat_axis=0, tiled=True
    ).reshape(slot_total, frames)
    owner_pick = (jnp.arange(neur_local, dtype=jnp.int32)[:, None] == asked_flat[None, :]).astype(
        jnp.float32
    )
    summed = jnp.dot(owner_pick, got_proj, precision=lax.Precision.HIGHEST)
    power = jnp.dot(owner_pick, got_power, precision=lax.Precision.HIGHEST)
    updated = jnp.maximum(
        0.0, traces.astype(jnp.float32) + summed / jnp.maximum(power, 0.5)[:, None]
    ).astype(jnp.bfloat16)
    slot_updated = slot_rows(updated)
    residual_two = residual_of(slot_updated)
    products = lax.dot_general(
        slot_updated, residual_two, (((1,), (1,)), ((), ())), preferred_element_type=jnp.float32
    ).reshape(slot_total, block_count, BLOCK)
    numerator = jnp.sum(jnp.where(block_pick[:, :, None], products, 0.0), axis=1)
    trace_power = jnp.sum(slot_updated.astype(jnp.float32) ** 2, axis=1)
    pl_rows = slot_total // BLOCK
    stacked = jnp.concatenate([numerator, trace_power.reshape(pl_rows, BLOCK)], axis=0)
    rows = stacked.shape[0]
    chunk = -(-rows // tm_count)
    stacked = jnp.pad(stacked, ((0, chunk * tm_count - rows), (0, 0)))
    parts = lax.all_to_all(
        stacked.reshape(tm_count, chunk, BLOCK), "tm", split_axis=0, concat_axis=0, tiled=True
    )
    mine = jnp.sum(parts, axis=0, keepdims=True)
    whole = lax.all_to_all(
        jnp.broadcast_to(mine, (tm_count, chunk, BLOCK)), "tm", split_axis=0, concat_axis=0, tiled=True
    ).reshape(chunk * tm_count, BLOCK)
    numer_all = whole[:slot_total]
    power_all = whole[slot_total : slot_total + pl_rows].reshape(slot_total)
    grown = jnp.maximum(0.0, masked.astype(jnp.float32) + numer_all / (power_all + 1e-06)[:, None])
    return (updated, jnp.where(usable[:, None], grown, 0.0))


def solution(mesh):
    return jax.shard_map(
        local,
        mesh=mesh,
        in_specs=(
            P("pix", "tm"),
            P("pix", "tm"),
            P("pix", None),
            P("pix"),
            P("pix"),
            P("pix", None),
        ),
        out_specs=(P("pix", "tm"), P("pix", None)),
        check_vma=False,
    )
```

```python
import jax
import jax.numpy as jnp
from jax import lax
from jax.sharding import PartitionSpec as P

BLOCK = 128


def local(movie, traces, footprints, slot_block, slot_neuron, bucket_fill):
    pix_count = lax.axis_size("pix")
    tm_count = lax.axis_size("tm")
    slot_total = footprints.shape[0]
    capacity = slot_total // pix_count
    neur_local = traces.shape[0]
    frames = traces.shape[1]
    block_count = movie.shape[0] // BLOCK
    usable_op = jnp.arange(capacity, dtype=jnp.int32)[None, :] < bucket_fill[0][:, None]
    masked_op = footprints.reshape(pix_count, capacity, BLOCK) * usable_op[:, :, None].astype(
        jnp.bfloat16
    )
    power_op = jnp.sum(masked_op.astype(jnp.float32) ** 2, axis=2)
    usable = usable_op.reshape(slot_total)
    masked = masked_op.reshape(slot_total, BLOCK)
    block_pick = slot_block[:, None] == jnp.arange(block_count, dtype=jnp.int32)[None, :]
    dense_map = (block_pick.astype(jnp.bfloat16)[:, :, None] * masked[:, None, :]).reshape(
        slot_total, block_count * BLOCK
    )
    asked = lax.all_to_all(
        slot_neuron.reshape(pix_count, capacity), "pix", split_axis=0, concat_axis=0, tiled=True
    )
    asked_flat = asked.reshape(slot_total)
    row_pick = (asked[:, :, None] == jnp.arange(neur_local, dtype=jnp.int32)[None, None, :]).astype(
        jnp.bfloat16
    )

    def slot_rows(source_rows):
        picked = jnp.einsum(
            "okn,nf->okf", row_pick, source_rows, preferred_element_type=jnp.float32
        ).astype(source_rows.dtype)
        got = lax.all_to_all(picked, "pix", split_axis=0, concat_axis=0, tiled=True)
        return got.reshape(slot_total, frames)

    def residual_of(slot_traces):
        rebuilt = lax.dot_general(
            dense_map, slot_traces, (((0,), (0,)), ((), ())), preferred_element_type=jnp.float32
        )
        return (movie.astype(jnp.float32) - rebuilt).astype(jnp.bfloat16)

    slot_traces = slot_rows(traces)
    residual = residual_of(slot_traces)
    projection = jnp.einsum(
        "okp,pf->okf",
        dense_map.reshape(pix_count, capacity, block_count * BLOCK),
        residual,
        preferred_element_type=jnp.float32,
    )
    got = lax.all_to_all(
        jnp.concatenate([projection.reshape(pix_count, capacity * frames), power_op], axis=1),
        "pix",
        split_axis=0,
        concat_axis=0,
        tiled=True,
    )
    got_proj = got[:, : capacity * frames].reshape(slot_total, frames)
    got_power = got[:, capacity * frames :].reshape(slot_total)
    owner_pick = (jnp.arange(neur_local, dtype=jnp.int32)[:, None] == asked_flat[None, :]).astype(
        jnp.float32
    )
    summed = jnp.dot(owner_pick, got_proj, precision=lax.Precision.HIGHEST)
    power = jnp.dot(owner_pick, got_power, precision=lax.Precision.HIGHEST)
    updated = jnp.maximum(
        0.0, traces.astype(jnp.float32) + summed / jnp.maximum(power, 0.5)[:, None]
    ).astype(jnp.bfloat16)
    slot_updated = slot_rows(updated)
    residual_two = residual_of(slot_updated)
    products = lax.dot_general(
        slot_updated, residual_two, (((1,), (1,)), ((), ())), preferred_element_type=jnp.float32
    ).reshape(slot_total, block_count, BLOCK)
    numerator = jnp.sum(jnp.where(block_pick[:, :, None], products, 0.0), axis=1)
    trace_power = jnp.sum(slot_updated.astype(jnp.float32) ** 2, axis=1)
    pl_rows = slot_total // BLOCK
    stacked = jnp.concatenate([numerator, trace_power.reshape(pl_rows, BLOCK)], axis=0)
    rows = stacked.shape[0]
    chunk = -(-rows // tm_count)
    stacked = jnp.pad(stacked, ((0, chunk * tm_count - rows), (0, 0)))
    parts = lax.all_to_all(
        stacked.reshape(tm_count, chunk, BLOCK), "tm", split_axis=0, concat_axis=0, tiled=True
    )
    mine = jnp.sum(parts, axis=0, keepdims=True)
    whole = lax.all_to_all(
        jnp.broadcast_to(mine, (tm_count, chunk, BLOCK)), "tm", split_axis=0, concat_axis=0, tiled=True
    ).reshape(chunk * tm_count, BLOCK)
    numer_all = whole[:slot_total]
    power_all = whole[slot_total : slot_total + pl_rows].reshape(slot_total)
    grown = jnp.maximum(0.0, masked.astype(jnp.float32) + numer_all / (power_all + 1e-06)[:, None])
    return (updated, jnp.where(usable[:, None], grown, 0.0))


def solution(mesh):
    return jax.shard_map(
        local,
        mesh=mesh,
        in_specs=(
            P("pix", "tm"),
            P("pix", "tm"),
            P("pix", None),
            P("pix"),
            P("pix"),
            P("pix", None),
        ),
        out_specs=(P("pix", "tm"), P("pix", None)),
        check_vma=False,
    )
```
